128 devices in a mesh: grp: 16 (over y, z), lag: 8 (over x, core).
Axes of the slice: x: 4, y: 4, z: 4, core: 2. Of those that a mesh axis runs over, the one named last changes fastest.
Arguments:
- history: float32 [16, 512, 32, 128], P('lag', 'grp'), may hold values from -6 to 6
- tiles: bfloat16 [65536, 128, 128], P(('grp', 'lag')), may hold values from -0.01171875 to 0.01171875
- tile_src: int32 [65536], P(('grp', 'lag')), may hold values from 0 to 511
- tile_obs: int32 [65536], P(('grp', 'lag')), may hold values from 0 to 32
- tile_lag: int32 [65536], P(('grp', 'lag')), may hold values from 0 to 1
- incident: float32 [32, 32, 128], P('grp', 'lag'), may hold values from -6 to 6
- near_inverse: bfloat16 [32, 128, 128], P('grp'), may hold values from -0.5 to 0.5
Outputs:
- field: float32 [32, 32, 128], P('grp', 'lag')
- new_current: float32 [32, 32, 128], P('grp', 'lag')
The draws below stay inside these ranges and needn't reach their ends.
Inputs may be any that keep to these rules, and one draw needn't show every extreme that they name: `tile_obs`: a value of 32 marks a padded tile.
All inputs are finite; a program needn't handle non-finite values.
Results may differ from the reference program's by a relative error of at most 0.0035.
Values may be sent and summed in bfloat16 or wider, within the bound.
No kernel may reach another device: no remote copies, remote signals or barrier semaphores. Data moves between devices by JAX's collectives and lax.ppermute only.
A program may use at most 128 MiB of HBM per device.

```python
import jax
import jax.numpy as jnp
from jax import lax

G = 128
A = 32
LAG_DEV = 2
TILES = 512
SRC = 512
OBS = 32
LAGS = 16
TILES_ALL = 65536
N_GRP = 16
N_LAG = 8


def set_ends(drawn, rng, smallest, top_value):
    longest = drawn.shape.index(max(drawn.shape))
    spots = []
    for shift in (0, 1):
        where = [jax.random.randint(jax.random.fold_in(rng, axis), (), 0, length) for axis, length in enumerate(drawn.shape)]
        where[longest] = (where[longest] + shift) % drawn.shape[longest]
        spots.append(tuple(where))
    return drawn.at[spots[0]].set(smallest).at[spots[1]].set(top_value)


def level_of(rng, shape, split, low, high):
    level = 1.0
    for dim, shards_of in split:
        steps = jax.random.uniform(jax.random.fold_in(jax.random.fold_in(rng, 6), dim), (shards_of,), jnp.float32, low / len(split), high / len(split))
        level = level * jnp.repeat(jnp.exp(steps), shape[dim] // shards_of).reshape((-1,) + (1,) * (len(shape) - 1 - dim))
    return level


def centred(rng, shape, deviation, reach, cuts=(), kind=jnp.bfloat16):
    array = deviation * jax.random.normal(rng, shape, jnp.float32)
    if cuts:
        array = array * level_of(rng, shape, cuts, -0.22, 0.18)
    return jnp.clip(array, -reach, reach).astype(kind)


def setup_inputs(seed: int = 0) -> dict:
    arg_keys = jax.random.split(jax.random.key(seed), 8)
    history = centred(arg_keys[0], (LAGS, SRC, A, G), 1.0, 6.0, ((0, 8), (1, 16)), jnp.float32)
    tiles = centred(arg_keys[1], (TILES_ALL, G, G), (G * TILES_ALL // OBS) ** -0.5, 0.01171875, ((0, 128),))
    tile_src = set_ends(jax.random.randint(arg_keys[2], (TILES_ALL,), 0, SRC), jax.random.fold_in(arg_keys[2], 1), 0, SRC - 1).astype(jnp.int32)
    tile_obs = set_ends(jax.random.randint(arg_keys[3], (TILES_ALL,), 0, OBS + 1), jax.random.fold_in(arg_keys[3], 1), 0, OBS).astype(jnp.int32)
    tile_lag = set_ends(jax.random.randint(arg_keys[4], (TILES_ALL,), 0, LAG_DEV), jax.random.fold_in(arg_keys[4], 1), 0, LAG_DEV - 1).astype(jnp.int32)
    incident = centred(arg_keys[5], (OBS, A, G), 1.0, 6.0, ((0, 16), (1, 8)), jnp.float32)
    near_inverse = centred(arg_keys[6], (OBS, G, G), G ** -0.5, 0.5, ((0, 16),))
    return dict(history=history, tiles=tiles, tile_src=tile_src, tile_obs=tile_obs, tile_lag=tile_lag, incident=incident, near_inverse=near_inverse)


def reference(history, tiles, tile_src, tile_obs, tile_lag, incident, near_inverse):
    hist16 = history.astype(jnp.bfloat16)
    flat = hist16.reshape(LAGS * SRC, A, G)
    blocks = N_GRP * N_LAG

    def one_block(total, block):
        start = (block * TILES).astype(jnp.int32)
        part_tiles = lax.dynamic_slice_in_dim(tiles, start, TILES, 0)
        sources = lax.dynamic_slice_in_dim(tile_src, start, TILES, 0)
        targets = lax.dynamic_slice_in_dim(tile_obs, start, TILES, 0)
        lags = lax.dynamic_slice_in_dim(tile_lag, start, TILES, 0)
        global_lag = (block % N_LAG).astype(jnp.int32) * LAG_DEV + lags
        picked = flat[(global_lag * SRC + sources).astype(jnp.int32)]
        terms = jnp.einsum("kas,kos->kao", picked.astype(jnp.float32), part_tiles.astype(jnp.float32))
        return total + jax.ops.segment_sum(terms, targets, num_segments=OBS), None

    start_total = jnp.zeros((OBS, A, G), jnp.float32)
    field, _ = lax.scan(one_block, start_total, jnp.arange(blocks, dtype=jnp.int32))
    rhs = (incident - field).astype(jnp.bfloat16)
    new_current = jnp.einsum("oag,ohg->oah", rhs.astype(jnp.float32), near_inverse.astype(jnp.float32))
    return field, new_current
```

```python
import jax
import jax.numpy as jnp
from jax import lax
from jax.sharding import PartitionSpec as P


def body(history, tiles, tile_src, tile_obs, tile_lag, incident, near_inverse):
    n_grp = lax.axis_size("grp")
    n_lag = lax.axis_size("lag")
    obs_dev, ang_dev, width = incident.shape
    observers = obs_dev * n_grp
    hist16 = history.astype(jnp.bfloat16)
    gathered = lax.all_gather(hist16, "grp", axis=1, tiled=True)
    lag_count = gathered.shape[0]
    source_count = gathered.shape[1]
    flat = gathered.reshape(lag_count * source_count, gathered.shape[2], gathered.shape[3])
    picked = flat[tile_lag * source_count + tile_src]
    terms = jnp.einsum("kas,kos->kao", picked, tiles, preferred_element_type=jnp.float32)
    onehot = (tile_obs[:, None] == jnp.arange(observers, dtype=tile_obs.dtype)[None, :]).astype(jnp.float32)
    partial = jnp.einsum("kg,kao->gao", onehot, terms, precision=lax.Precision.HIGHEST,
                         preferred_element_type=jnp.float32)
    partial = partial.reshape(n_grp, obs_dev, n_lag, ang_dev, width)
    partial = partial.transpose(0, 2, 1, 3, 4).reshape(n_grp * n_lag, obs_dev, ang_dev, width)
    field = lax.psum_scatter(partial, ("grp", "lag"), scatter_dimension=0, tiled=True)[0]
    rhs = (incident - field).astype(jnp.bfloat16)
    new_current = jnp.einsum("oag,ohg->oah", rhs, near_inverse, preferred_element_type=jnp.float32)
    return (field, new_current)


def solution(mesh):
    return jax.shard_map(
        body,
        mesh=mesh,
        in_specs=(
            P("lag", "grp", None, None),
            P(("grp", "lag"), None, None),
            P(("grp", "lag")),
            P(("grp", "lag")),
            P(("grp", "lag")),
            P("grp", "lag", None),
            P("grp", None, None),
        ),
        out_specs=(P("grp", "lag", None), P("grp", "lag", None)),
        check_vma=False,
    )
```

```python
import jax
import jax.numpy as jnp
from jax import lax
from jax.sharding import PartitionSpec as P


def body(history, tiles, tile_src, tile_obs, tile_lag, incident, near_inverse):
    n_grp = lax.axis_size("grp")
    n_lag = lax.axis_size("lag")
    obs_dev, ang_dev, width = incident.shape
    observers = obs_dev * n_grp
    hist16 = history.astype(jnp.bfloat16)
    gathered = lax.all_gather(hist16, "grp", axis=1, tiled=True)
    lag_count = gathered.shape[0]
    source_count = gathered.shape[1]
    flat = gathered.reshape(lag_count * source_count, gathered.shape[2], gathered.shape[3])
    picked = flat[tile_lag * source_count + tile_src]
    terms = jnp.einsum("kas,kos->kao", picked, tiles, preferred_element_type=jnp.float32)
    onehot = (tile_obs[:, None] == jnp.arange(observers, dtype=tile_obs.dtype)[None, :]).astype(jnp.float32)
    partial = jnp.einsum("kg,kao->gao", onehot, terms, precision=lax.Precision.HIGHEST,
                         preferred_element_type=jnp.float32)
    partial = partial.reshape(n_grp, obs_dev, n_lag, ang_dev, width)
    partial = partial.transpose(0, 2, 1, 3, 4).reshape(n_grp * n_lag, obs_dev, ang_dev, width)
    received = lax.all_to_all(partial, ("grp", "lag"), 0, 0, tiled=True)
    field = jnp.sum(received, axis=0)
    rhs = (incident - field).astype(jnp.bfloat16)
    new_current = jnp.einsum("oag,ohg->oah", rhs, near_inverse, preferred_element_type=jnp.float32)
    return (field, new_current)


def solution(mesh):
    return jax.shard_map(
        body,
        mesh=mesh,
        in_specs=(
            P("lag", "grp", None, None),
            P(("grp", "lag"), None, None),
            P(("grp", "lag")),
            P(("grp", "lag")),
            P(("grp", "lag")),
            P("grp", "lag", None),
            P("grp", None, None),
        ),
        out_specs=(P("grp", "lag", None), P("grp", "lag", None)),
        check_vma=False,
    )
```

```python
import jax
import jax.numpy as jnp
from jax import lax
from jax.sharding import PartitionSpec as P

CHUNKS = 2


def chunk_field(hist16, tile_index, tiles, onehot, n_grp, n_lag, obs_dev):
    gathered = lax.all_gather(hist16, "grp", axis=1, tiled=True)
    lag_count, source_count, angles, width = gathered.shape
    flat = gathered.reshape(lag_count * source_count, angles, width)
    picked = flat[tile_index]
    terms = jnp.einsum("kas,kos->kao", picked, tiles, preferred_element_type=jnp.float32)
    partial = jnp.einsum("kg,kao->gao", onehot, terms, precision=lax.Precision.HIGHEST,
                         preferred_element_type=jnp.float32)
    per_lag = angles // n_lag
    partial = partial.reshape(n_grp, obs_dev, n_lag, per_lag, width)
    partial = partial.transpose(0, 2, 1, 3, 4).reshape(n_grp * n_lag, obs_dev, per_lag, width)
    received = lax.all_to_all(partial, ("grp", "lag"), 0, 0, tiled=True)
    return jnp.sum(received, axis=0)


def body(history, tiles, tile_src, tile_obs, tile_lag, incident, near_inverse):
    n_grp = lax.axis_size("grp")
    n_lag = lax.axis_size("lag")
    obs_dev, ang_dev, width = incident.shape
    observers = obs_dev * n_grp
    lag_count, src_dev, angles, _ = history.shape
    source_count = src_dev * n_grp
    tile_index = tile_lag * source_count + tile_src
    onehot = (tile_obs[:, None] == jnp.arange(observers, dtype=tile_obs.dtype)[None, :]).astype(jnp.float32)
    split = history.reshape(lag_count, src_dev, n_lag, CHUNKS, ang_dev // CHUNKS, width)
    fields = []
    for c in range(CHUNKS):
        part = split[:, :, :, c].reshape(lag_count, src_dev, angles // CHUNKS, width)
        fields.append(chunk_field(part.astype(jnp.bfloat16), tile_index, tiles, onehot, n_grp, n_lag, obs_dev))
    field = jnp.concatenate(fields, axis=1)
    rhs = (incident - field).astype(jnp.bfloat16)
    new_current = jnp.einsum("oag,ohg->oah", rhs, near_inverse, preferred_element_type=jnp.float32)
    return (field, new_current)


def solution(mesh):
    return jax.shard_map(
        body,
        mesh=mesh,
        in_specs=(
            P("lag", "grp", None, None),
            P(("grp", "lag"), None, None),
            P(("grp", "lag")),
            P(("grp", "lag")),
            P(("grp", "lag")),
            P("grp", "lag", None),
            P("grp", None, None),
        ),
        out_specs=(P("grp", "lag", None), P("grp", "lag", None)),
        check_vma=False,
    )
```

```python
import jax
import jax.numpy as jnp
from jax import lax
from jax.sharding import PartitionSpec as P


def shift_pairs(rows, cols, step, along_cols):
    pairs = []
    for a in range(rows):
        for b in range(cols):
            if along_cols:
                pairs.append((a * cols + b, a * cols + (b + step) % cols))
            else:
                pairs.append((a * cols + b, ((a + step) % rows) * cols + b))
    return pairs


def ring_gather(x, rows, cols, along_cols):
    n = cols if along_cols else rows
    plus = shift_pairs(rows, cols, 1, along_cols)
    minus = shift_pairs(rows, cols, -1, along_cols)
    from_behind = lax.ppermute(x, "grp", plus)
    from_ahead = lax.ppermute(x, "grp", minus)
    assert n == 4
    half = x.shape[0] // 2
    far_a = lax.ppermute(from_behind[:half], "grp", plus)
    far_b = lax.ppermute(from_ahead[half:], "grp", minus)
    far = jnp.concatenate([far_a, far_b], axis=0)
    return jnp.stack([x, from_ahead, far, from_behind])


def body(history, tiles, tile_src, tile_obs, tile_lag, incident, near_inverse):
    n_grp = lax.axis_size("grp")
    n_lag = lax.axis_size("lag")
    obs_dev, ang_dev, width = incident.shape
    observers = obs_dev * n_grp
    hist16 = history.astype(jnp.bfloat16)
    lag_count, src_dev, angles, _ = hist16.shape
    rows = 4
    cols = n_grp // rows
    assert lag_count == 2 and rows * cols == n_grp
    first = ring_gather(ring_gather(hist16[0], rows, cols, True), rows, cols, False)
    second = ring_gather(ring_gather(hist16[1], rows, cols, False), rows, cols, True)
    per_lag = n_grp * src_dev
    flat = jnp.concatenate([first.reshape(per_lag, angles, width), second.reshape(per_lag, angles, width)])
    me = lax.axis_index("grp")
    owner = tile_src // src_dev
    local = tile_src % src_dev
    dy = (owner // cols - me // cols + rows) % rows
    dz = (owner % cols - me % cols + cols) % cols
    index_first = (dy * cols + dz) * src_dev + local
    index_second = per_lag + (dz * rows + dy) * src_dev + local
    picked = flat[jnp.where(tile_lag == 0, index_first, index_second)]
    terms = jnp.einsum("kas,kos->kao", picked, tiles, preferred_element_type=jnp.float32)
    onehot = (tile_obs[:, None] == jnp.arange(observers, dtype=tile_obs.dtype)[None, :]).astype(jnp.float32)
    partial = jnp.einsum("kg,kao->gao", onehot, terms, precision=lax.Precision.HIGHEST,
                         preferred_element_type=jnp.float32)
    partial = partial.reshape(n_grp, obs_dev, n_lag, ang_dev, width)
    partial = partial.transpose(0, 2, 1, 3, 4).reshape(n_grp * n_lag, obs_dev, ang_dev, width)
    received = lax.all_to_all(partial, ("grp", "lag"), 0, 0, tiled=True)
    field = jnp.sum(received, axis=0)
    rhs = (incident - field).astype(jnp.bfloat16)
    new_current = jnp.einsum("oag,ohg->oah", rhs, near_inverse, preferred_element_type=jnp.float32)
    return (field, new_current)


def solution(mesh):
    return jax.shard_map(
        body,
        mesh=mesh,
        in_specs=(
            P("lag", "grp", None, None),
            P(("grp", "lag"), None, None),
            P(("grp", "lag")),
            P(("grp", "lag")),
            P(("grp", "lag")),
            P("grp", "lag", None),
            P("grp", None, None),
        ),
        out_specs=(P("grp", "lag", None), P("grp", "lag", None)),
        check_vma=False,
    )
```

```python
import jax
import jax.numpy as jnp
from jax import lax
from jax.sharding import PartitionSpec as P


def body(history, tiles, tile_src, tile_obs, tile_lag, incident, near_inverse):
    n_grp = lax.axis_size("grp")
    n_lag = lax.axis_size("lag")
    obs_dev, ang_dev, width = incident.shape
    observers = obs_dev * n_grp
    hist16 = history.astype(jnp.bfloat16)
    gathered = lax.all_gather(hist16, "grp", axis=1, tiled=True)
    lag_count = gathered.shape[0]
    source_count = gathered.shape[1]
    flat = gathered.reshape(lag_count * source_count, gathered.shape[2], gathered.shape[3])
    picked = flat[tile_lag * source_count + tile_src]
    terms = jnp.einsum("kas,kos->kao", picked, tiles, preferred_element_type=jnp.float32)
    onehot = (tile_obs[:, None] == jnp.arange(observers, dtype=tile_obs.dtype)[None, :]).astype(jnp.bfloat16)
    high = terms.astype(jnp.bfloat16)
    low = (terms - high.astype(jnp.float32)).astype(jnp.bfloat16)
    partial = (jnp.einsum("kg,kao->gao", onehot, high, preferred_element_type=jnp.float32)
               + jnp.einsum("kg,kao->gao", onehot, low, preferred_element_type=jnp.float32))
    partial = partial.reshape(n_grp, obs_dev, n_lag, ang_dev, width)
    by_grp = lax.all_to_all(partial, "grp", 0, 0, tiled=True)
    partial = jnp.sum(by_grp, axis=0).transpose(1, 0, 2, 3)
    by_lag = lax.all_to_all(partial, "lag", 0, 0, tiled=True)
    field = jnp.sum(by_lag, axis=0)
    rhs = (incident - field).astype(jnp.bfloat16)
    new_current = jnp.einsum("oag,ohg->oah", rhs, near_inverse, preferred_element_type=jnp.float32)
    return (field, new_current)


def solution(mesh):
    return jax.shard_map(
        body,
        mesh=mesh,
        in_specs=(
            P("lag", "grp", None, None),
            P(("grp", "lag"), None, None),
            P(("grp", "lag")),
            P(("grp", "lag")),
            P(("grp", "lag")),
            P("grp", "lag", None),
            P("grp", None, None),
        ),
        out_specs=(P("grp", "lag", None), P("grp", "lag", None)),
        check_vma=False,
    )
```

```python
import jax
import jax.numpy as jnp
from jax import lax
from jax.sharding import PartitionSpec as P


def body(history, tiles, tile_src, tile_obs, tile_lag, incident, near_inverse):
    n_grp = lax.axis_size("grp")
    n_lag = lax.axis_size("lag")
    obs_dev, ang_dev, width = incident.shape
    observers = obs_dev * n_grp
    hist16 = history.astype(jnp.bfloat16)
    gathered = lax.all_gather(hist16, "grp", axis=1, tiled=True)
    lag_count = gathered.shape[0]
    source_count = gathered.shape[1]
    flat = gathered.reshape(lag_count * source_count, gathered.shape[2], gathered.shape[3])
    picked = flat[tile_lag * source_count + tile_src]
    terms = jnp.einsum("kas,kos->kao", picked, tiles, preferred_element_type=jnp.float32)
    onehot = (tile_obs[:, None] == jnp.arange(observers, dtype=tile_obs.dtype)[None, :]).astype(jnp.float32)
    partial = jnp.einsum("kg,kao->gao", onehot, terms, precision=lax.Precision.HIGH,
                         preferred_element_type=jnp.float32)
    partial = partial.reshape(n_grp, obs_dev, n_lag, ang_dev, width)
    partial = partial.transpose(0, 2, 1, 3, 4).reshape(n_grp * n_lag, obs_dev, ang_dev, width)
    received = lax.all_to_all(partial, ("grp", "lag"), 0, 0, tiled=True)
    field = jnp.sum(received, axis=0)
    rhs = (incident - field).astype(jnp.bfloat16)
    new_current = jnp.einsum("oag,ohg->oah", rhs, near_inverse, preferred_element_type=jnp.float32)
    return (field, new_current)


def solution(mesh):
    return jax.shard_map(
        body,
        mesh=mesh,
        in_specs=(
            P("lag", "grp", None, None),
            P(("grp", "lag"), None, None),
            P(("grp", "lag")),
            P(("grp", "lag")),
            P(("grp", "lag")),
            P("grp", "lag", None),
            P("grp", None, None),
        ),
        out_specs=(P("grp", "lag", None), P("grp", "lag", None)),
        check_vma=False,
    )
```

```python
import jax
import jax.numpy as jnp
from jax import lax
from jax.experimental import pallas as pl
from jax.experimental.pallas import tpu as pltpu
from jax.sharding import PartitionSpec as P

BLOCK = 32


def field_kernel(index_ref, obs_ref, table_ref, tiles_ref, out_ref, rows, acc, sems):
    step = pl.program_id(0)
    steps = pl.num_programs(0)
    block = tiles_ref.shape[0]

    def fetch(which, slot):
        for t in range(block):
            pltpu.make_async_copy(table_ref.at[index_ref[which * block + t]], rows.at[slot, t], sems.at[slot]).start()

    def wait(slot):
        for t in range(block):
            pltpu.make_async_copy(table_ref.at[0], rows.at[slot, t], sems.at[slot]).wait()

    slot = step % 2

    @pl.when(step == 0)
    def _():
        acc[...] = jnp.zeros_like(acc)
        fetch(0, 0)

    wait(slot)

    @pl.when(step + 1 < steps)
    def _():
        fetch(step + 1, 1 - slot)

    def one(t, carry):
        term = lax.dot_general(rows[slot, t], tiles_ref[t], (((1,), (1,)), ((), ())),
                               preferred_element_type=jnp.float32)
        o = obs_ref[step * block + t]
        acc[o] = acc[o] + term
        return carry

    lax.fori_loop(0, block, one, 0, unroll=8)

    @pl.when(step == steps - 1)
    def _():
        out_ref[...] = acc[: out_ref.shape[0]]


def field_partial(table, tile_index, tile_obs, tiles, observers):
    count, angles, width = table.shape
    n_tiles = tiles.shape[0]
    grid_spec = pltpu.PrefetchScalarGridSpec(
        num_scalar_prefetch=2,
        grid=(n_tiles // BLOCK,),
        in_specs=[
            pl.BlockSpec(memory_space=pl.ANY),
            pl.BlockSpec((BLOCK,) + tiles.shape[1:], lambda i, *_: (i, 0, 0)),
        ],
        out_specs=pl.BlockSpec((observers, angles, width), lambda i, *_: (0, 0, 0)),
        scratch_shapes=[
            pltpu.VMEM((2, BLOCK, angles, width), table.dtype),
            pltpu.VMEM((observers + 1, angles, width), jnp.float32),
            pltpu.SemaphoreType.DMA((2,)),
        ],
    )
    return pl.pallas_call(
        field_kernel,
        grid_spec=grid_spec,
        out_shape=jax.ShapeDtypeStruct((observers, angles, width), jnp.float32),
        compiler_params=pltpu.CompilerParams(dimension_semantics=("arbitrary",)),
    )(tile_index, tile_obs, table, tiles)


def body(history, tiles, tile_src, tile_obs, tile_lag, incident, near_inverse):
    n_grp = lax.axis_size("grp")
    n_lag = lax.axis_size("lag")
    obs_dev, ang_dev, width = incident.shape
    observers = obs_dev * n_grp
    hist16 = history.astype(jnp.bfloat16)
    gathered = lax.all_gather(hist16, "grp", axis=1, tiled=True)
    lag_count = gathered.shape[0]
    source_count = gathered.shape[1]
    flat = gathered.reshape(lag_count * source_count, gathered.shape[2], gathered.shape[3])
    tile_index = tile_lag * source_count + tile_src
    partial = field_partial(flat, tile_index, tile_obs, tiles, observers)
    partial = partial.reshape(n_grp, obs_dev, n_lag, ang_dev, width)
    partial = partial.transpose(0, 2, 1, 3, 4).reshape(n_grp * n_lag, obs_dev, ang_dev, width)
    received = lax.all_to_all(partial, ("grp", "lag"), 0, 0, tiled=True)
    field = jnp.sum(received, axis=0)
    rhs = (incident - field).astype(jnp.bfloat16)
    new_current = jnp.einsum("oag,ohg->oah", rhs, near_inverse, preferred_element_type=jnp.float32)
    return (field, new_current)


def solution(mesh):
    return jax.shard_map(
        body,
        mesh=mesh,
        in_specs=(
            P("lag", "grp", None, None),
            P(("grp", "lag"), None, None),
            P(("grp", "lag")),
            P(("grp", "lag")),
            P(("grp", "lag")),
            P("grp", "lag", None),
            P("grp", None, None),
        ),
        out_specs=(P("grp", "lag", None), P("grp", "lag", None)),
        check_vma=False,
    )
```

```python
import jax
import jax.numpy as jnp
from jax import lax
from jax.experimental import pallas as pl
from jax.experimental.pallas import tpu as pltpu
from jax.sharding import PartitionSpec as P

BLOCK = 128


def field_kernel(index_ref, obs_ref, table_ref, tiles_ref, out_ref, rows, acc, sems):
    step = pl.program_id(0)
    steps = pl.num_programs(0)
    block = tiles_ref.shape[0]

    def fetch(which, slot):
        for t in range(block):
            pltpu.make_async_copy(table_ref.at[index_ref[which * block + t]], rows.at[slot, t], sems.at[slot]).start()

    def wait(slot):
        for t in range(block):
            pltpu.make_async_copy(table_ref.at[0], rows.at[slot, t], sems.at[slot]).wait()

    slot = step % 2

    @pl.when(step == 0)
    def _():
        acc[...] = jnp.zeros_like(acc)
        fetch(0, 0)

    wait(slot)

    @pl.when(step + 1 < steps)
    def _():
        fetch(step + 1, 1 - slot)

    def one(t, carry):
        term = lax.dot_general(rows[slot, t], tiles_ref[t], (((1,), (1,)), ((), ())),
                               preferred_element_type=jnp.float32)
        o = obs_ref[step * block + t]
        acc[o] = acc[o] + term
        return carry

    lax.fori_loop(0, block, one, 0, unroll=32)

    @pl.when(step == steps - 1)
    def _():
        out_ref[...] = acc[: out_ref.shape[0]]


def field_partial(table, tile_index, tile_obs, tiles, observers):
    count, angles, width = table.shape
    n_tiles = tiles.shape[0]
    grid_spec = pltpu.PrefetchScalarGridSpec(
        num_scalar_prefetch=2,
        grid=(n_tiles // BLOCK,),
        in_specs=[
            pl.BlockSpec(memory_space=pl.ANY),
            pl.BlockSpec((BLOCK,) + tiles.shape[1:], lambda i, *_: (i, 0, 0)),
        ],
        out_specs=pl.BlockSpec((observers, angles, width), lambda i, *_: (0, 0, 0)),
        scratch_shapes=[
            pltpu.VMEM((2, BLOCK, angles, width), table.dtype),
            pltpu.VMEM((observers + 1, angles, width), jnp.float32),
            pltpu.SemaphoreType.DMA((2,)),
        ],
    )
    return pl.pallas_call(
        field_kernel,
        grid_spec=grid_spec,
        out_shape=jax.ShapeDtypeStruct((observers, angles, width), jnp.float32),
        compiler_params=pltpu.CompilerParams(dimension_semantics=("arbitrary",)),
    )(tile_index, tile_obs, table, tiles)


def body(history, tiles, tile_src, tile_obs, tile_lag, incident, near_inverse):
    n_grp = lax.axis_size("grp")
    n_lag = lax.axis_size("lag")
    obs_dev, ang_dev, width = incident.shape
    observers = obs_dev * n_grp
    hist16 = history.astype(jnp.bfloat16)
    lag_count, src_dev, angles, _ = hist16.shape
    flat = lax.all_gather(hist16.reshape(lag_count * src_dev, angles, width), "grp", axis=0, tiled=True)
    owner = tile_src // src_dev
    tile_index = (owner * lag_count + tile_lag) * src_dev + tile_src % src_dev
    partial = field_partial(flat, tile_index, tile_obs, tiles, observers)
    partial = partial.reshape(n_grp, obs_dev, n_lag, ang_dev, width)
    partial = partial.transpose(0, 2, 1, 3, 4).reshape(n_grp * n_lag, obs_dev, ang_dev, width)
    received = lax.all_to_all(partial, ("grp", "lag"), 0, 0, tiled=True)
    field = jnp.sum(received, axis=0)
    rhs = (incident - field).astype(jnp.bfloat16)
    new_current = jnp.einsum("oag,ohg->oah", rhs, near_inverse, preferred_element_type=jnp.float32)
    return (field, new_current)


def solution(mesh):
    return jax.shard_map(
        body,
        mesh=mesh,
        in_specs=(
            P("lag", "grp", None, None),
            P(("grp", "lag"), None, None),
            P(("grp", "lag")),
            P(("grp", "lag")),
            P(("grp", "lag")),
            P("grp", "lag", None),
            P("grp", None, None),
        ),
        out_specs=(P("grp", "lag", None), P("grp", "lag", None)),
        check_vma=False,
    )
```

```python
import jax
import jax.numpy as jnp
from jax import lax
from jax.experimental import pallas as pl
from jax.experimental.pallas import tpu as pltpu
from jax.sharding import PartitionSpec as P

BLOCK = 128


def field_kernel(index_ref, lag_ref, obs_ref, table_ref, other_ref, tiles_ref, out_ref, rows, acc, sems):
    step = pl.program_id(0)
    steps = pl.num_programs(0)
    block = tiles_ref.shape[0]

    def fetch(which, slot):
        def issue(t, carry):
            r = which * block + t
            i = index_ref[r]

            @pl.when(lag_ref[r] == 0)
            def _():
                pltpu.make_async_copy(table_ref.at[i], rows.at[slot, t], sems.at[slot]).start()

            @pl.when(lag_ref[r] != 0)
            def _():
                pltpu.make_async_copy(other_ref.at[i], rows.at[slot, t], sems.at[slot]).start()

            return carry

        lax.fori_loop(0, block, issue, 0, unroll=8)

    def wait(slot):
        def one_wait(t, carry):
            pltpu.make_async_copy(table_ref.at[0], rows.at[slot, t], sems.at[slot]).wait()
            return carry

        lax.fori_loop(0, block, one_wait, 0, unroll=8)

    slot = step % 2

    @pl.when(step == 0)
    def _():
        acc[...] = jnp.zeros_like(acc)
        fetch(0, 0)

    wait(slot)

    @pl.when(step + 1 < steps)
    def _():
        fetch(step + 1, 1 - slot)

    def one(t, carry):
        term = lax.dot_general(rows[slot, t], tiles_ref[t], (((1,), (1,)), ((), ())),
                               preferred_element_type=jnp.float32)
        o = obs_ref[step * block + t]
        acc[o] = acc[o] + term
        return carry

    lax.fori_loop(0, block, one, 0, unroll=32)

    @pl.when(step == steps - 1)
    def _():
        out_ref[...] = acc[: out_ref.shape[0]]


def field_partial(table, other, tile_index, tile_lag, tile_obs, tiles, observers):
    count, angles, width = table.shape
    n_tiles = tiles.shape[0]
    grid_spec = pltpu.PrefetchScalarGridSpec(
        num_scalar_prefetch=3,
        grid=(n_tiles // BLOCK,),
        in_specs=[
            pl.BlockSpec(memory_space=pl.ANY),
            pl.BlockSpec(memory_space=pl.ANY),
            pl.BlockSpec((BLOCK,) + tiles.shape[1:], lambda i, *_: (i, 0, 0)),
        ],
        out_specs=pl.BlockSpec((observers, angles, width), lambda i, *_: (0, 0, 0)),
        scratch_shapes=[
            pltpu.VMEM((2, BLOCK, angles, width), table.dtype),
            pltpu.VMEM((observers + 1, angles, width), jnp.float32),
            pltpu.SemaphoreType.DMA((2,)),
        ],
    )
    return pl.pallas_call(
        field_kernel,
        grid_spec=grid_spec,
        out_shape=jax.ShapeDtypeStruct((observers, angles, width), jnp.float32),
        compiler_params=pltpu.CompilerParams(dimension_semantics=("arbitrary",)),
    )(tile_index, tile_lag, tile_obs, table, other, tiles)


def shift_pairs(rows, cols, step, along_cols):
    pairs = []
    for a in range(rows):
        for b in range(cols):
            if along_cols:
                pairs.append((a * cols + b, a * cols + (b + step) % cols))
            else:
                pairs.append((a * cols + b, ((a + step) % rows) * cols + b))
    return pairs


def ring_gather(x, rows, cols, along_cols):
    n = cols if along_cols else rows
    plus = shift_pairs(rows, cols, 1, along_cols)
    minus = shift_pairs(rows, cols, -1, along_cols)
    from_behind = lax.ppermute(x, "grp", plus)
    from_ahead = lax.ppermute(x, "grp", minus)
    assert n == 4
    half = x.shape[0] // 2
    far_a = lax.ppermute(from_behind[:half], "grp", plus)
    far_b = lax.ppermute(from_ahead[half:], "grp", minus)
    far = jnp.concatenate([far_a, far_b], axis=0)
    return jnp.stack([x, from_ahead, far, from_behind])


def body(history, tiles, tile_src, tile_obs, tile_lag, incident, near_inverse):
    n_grp = lax.axis_size("grp")
    n_lag = lax.axis_size("lag")
    obs_dev, ang_dev, width = incident.shape
    observers = obs_dev * n_grp
    hist16 = history.astype(jnp.bfloat16)
    lag_count, src_dev, angles, _ = hist16.shape
    rows = 4
    cols = n_grp // rows
    assert lag_count == 2 and rows * cols == n_grp
    table = lax.all_gather(hist16[0], "grp", axis=0, tiled=True)
    other = ring_gather(ring_gather(hist16[1], rows, cols, True), rows, cols, False)
    other = other.reshape(n_grp * src_dev, angles, width)
    me = lax.axis_index("grp")
    owner = tile_src // src_dev
    dy = (owner // cols - me // cols + rows) % rows
    dz = (owner % cols - me % cols + cols) % cols
    other_index = (dy * cols + dz) * src_dev + tile_src % src_dev
    tile_index = jnp.where(tile_lag == 0, tile_src, other_index)
    partial = field_partial(table, other, tile_index, tile_lag, tile_obs, tiles, observers)
    partial = partial.reshape(n_grp, obs_dev, n_lag, ang_dev, width)
    partial = partial.transpose(0, 2, 1, 3, 4).reshape(n_grp * n_lag, obs_dev, ang_dev, width)
    received = lax.all_to_all(partial, ("grp", "lag"), 0, 0, tiled=True)
    field = jnp.sum(received, axis=0)
    rhs = (incident - field).astype(jnp.bfloat16)
    new_current = jnp.einsum("oag,ohg->oah", rhs, near_inverse, preferred_element_type=jnp.float32)
    return (field, new_current)


def solution(mesh):
    return jax.shard_map(
        body,
        mesh=mesh,
        in_specs=(
            P("lag", "grp", None, None),
            P(("grp", "lag"), None, None),
            P(("grp", "lag")),
            P(("grp", "lag")),
            P(("grp", "lag")),
            P("grp", "lag", None),
            P("grp", None, None),
        ),
        out_specs=(P("grp", "lag", None), P("grp", "lag", None)),
        check_vma=False,
    )
```

```python
import jax
import jax.numpy as jnp
from jax import lax
from jax.experimental import pallas as pl
from jax.experimental.pallas import tpu as pltpu
from jax.sharding import PartitionSpec as P

BLOCK = 128


def field_kernel(index_ref, lag_ref, obs_ref, table_ref, other_ref, tiles_ref, out_ref, rows, acc, sems):
    step = pl.program_id(0)
    steps = pl.num_programs(0)
    block = tiles_ref.shape[0]

    def fetch(which, slot):
        def issue(t, carry):
            r = which * block + t
            i = index_ref[r]

            @pl.when(lag_ref[r] == 0)
            def _():
                pltpu.make_async_copy(table_ref.at[i], rows.at[slot, t], sems.at[slot]).start()

            @pl.when(lag_ref[r] != 0)
            def _():
                pltpu.make_async_copy(other_ref.at[i], rows.at[slot, t], sems.at[slot]).start()

            return carry

        lax.fori_loop(0, block, issue, 0, unroll=8)

    def wait(slot):
        def one_wait(t, carry):
            pltpu.make_async_copy(table_ref.at[0], rows.at[slot, t], sems.at[slot]).wait()
            return carry

        lax.fori_loop(0, block, one_wait, 0, unroll=8)

    slot = step % 2

    @pl.when(step == 0)
    def _():
        acc[...] = jnp.zeros_like(acc)
        fetch(0, 0)

    wait(slot)

    @pl.when(step + 1 < steps)
    def _():
        fetch(step + 1, 1 - slot)

    def one(t, carry):
        term = lax.dot_general(rows[slot, t], tiles_ref[t], (((1,), (1,)), ((), ())),
                               preferred_element_type=jnp.float32)
        o = obs_ref[step * block + t]
        acc[o] = acc[o] + term
        return carry

    lax.fori_loop(0, block, one, 0, unroll=32)

    @pl.when(step == steps - 1)
    def _():
        out_ref[...] = acc[: out_ref.shape[0]]


def field_partial(table, other, tile_index, tile_lag, tile_obs, tiles, observers):
    count, angles, width = table.shape
    n_tiles = tiles.shape[0]
    grid_spec = pltpu.PrefetchScalarGridSpec(
        num_scalar_prefetch=3,
        grid=(n_tiles // BLOCK,),
        in_specs=[
            pl.BlockSpec(memory_space=pl.ANY),
            pl.BlockSpec(memory_space=pl.ANY),
            pl.BlockSpec((BLOCK,) + tiles.shape[1:], lambda i, *_: (i, 0, 0)),
        ],
        out_specs=pl.BlockSpec((observers, angles, width), lambda i, *_: (0, 0, 0)),
        scratch_shapes=[
            pltpu.VMEM((2, BLOCK, angles, width), table.dtype),
            pltpu.VMEM((observers + 1, angles, width), jnp.float32),
            pltpu.SemaphoreType.DMA((2,)),
        ],
    )
    return pl.pallas_call(
        field_kernel,
        grid_spec=grid_spec,
        out_shape=jax.ShapeDtypeStruct((observers, angles, width), jnp.float32),
        compiler_params=pltpu.CompilerParams(dimension_semantics=("arbitrary",)),
    )(tile_index, tile_lag, tile_obs, table, other, tiles)


def shift_pairs(rows, cols, step, along_cols):
    pairs = []
    for a in range(rows):
        for b in range(cols):
            if along_cols:
                pairs.append((a * cols + b, a * cols + (b + step) % cols))
            else:
                pairs.append((a * cols + b, ((a + step) % rows) * cols + b))
    return pairs


def ring_gather(x, rows, cols, along_cols):
    n = cols if along_cols else rows
    plus = shift_pairs(rows, cols, 1, along_cols)
    minus = shift_pairs(rows, cols, -1, along_cols)
    from_behind = lax.ppermute(x, "grp", plus)
    from_ahead = lax.ppermute(x, "grp", minus)
    assert n == 4
    half = x.shape[0] // 2
    far_a = lax.ppermute(from_behind[:half], "grp", plus)
    far_b = lax.ppermute(from_ahead[half:], "grp", minus)
    far = jnp.concatenate([far_a, far_b], axis=0)
    return jnp.stack([x, from_ahead, far, from_behind])


def body(history, tiles, tile_src, tile_obs, tile_lag, incident, near_inverse):
    n_grp = lax.axis_size("grp")
    n_lag = lax.axis_size("lag")
    obs_dev, ang_dev, width = incident.shape
    observers = obs_dev * n_grp
    hist16 = history.astype(jnp.bfloat16)
    lag_count, src_dev, angles, _ = hist16.shape
    rows = 4
    cols = n_grp // rows
    assert lag_count == 2 and rows * cols == n_grp
    table = ring_gather(ring_gather(hist16[0], rows, cols, True), rows, cols, False)
    table = table.reshape(n_grp * src_dev, angles, width)
    other = ring_gather(ring_gather(hist16[1], rows, cols, False), rows, cols, True)
    other = other.reshape(n_grp * src_dev, angles, width)
    me = lax.axis_index("grp")
    owner = tile_src // src_dev
    local = tile_src % src_dev
    dy = (owner // cols - me // cols + rows) % rows
    dz = (owner % cols - me % cols + cols) % cols
    tile_index = jnp.where(tile_lag == 0, (dy * cols + dz) * src_dev + local, (dz * rows + dy) * src_dev + local)
    partial = field_partial(table, other, tile_index, tile_lag, tile_obs, tiles, observers)
    partial = partial.reshape(n_grp, obs_dev, n_lag, ang_dev, width)
    partial = partial.transpose(0, 2, 1, 3, 4).reshape(n_grp * n_lag, obs_dev, ang_dev, width)
    received = lax.all_to_all(partial, ("grp", "lag"), 0, 0, tiled=True)
    field = jnp.sum(received, axis=0)
    rhs = (incident - field).astype(jnp.bfloat16)
    new_current = jnp.einsum("oag,ohg->oah", rhs, near_inverse, preferred_element_type=jnp.float32)
    return (field, new_current)


def solution(mesh):
    return jax.shard_map(
        body,
        mesh=mesh,
        in_specs=(
            P("lag", "grp", None, None),
            P(("grp", "lag"), None, None),
            P(("grp", "lag")),
            P(("grp", "lag")),
            P(("grp", "lag")),
            P("grp", "lag", None),
            P("grp", None, None),
        ),
        out_specs=(P("grp", "lag", None), P("grp", "lag", None)),
        check_vma=False,
    )
```

```python
import jax
import jax.numpy as jnp
from jax import lax
from jax.experimental import pallas as pl
from jax.experimental.pallas import tpu as pltpu
from jax.sharding import PartitionSpec as P

BLOCK = 128


def field_kernel(index_ref, lag_ref, obs_ref, table_ref, other_ref, tiles_ref, out_ref, rows, acc, sems):
    step = pl.program_id(0)
    steps = pl.num_programs(0)
    block = tiles_ref.shape[0]

    def fetch(which, slot):
        def issue(t, carry):
            r = which * block + t
            i = index_ref[r]

            @pl.when(lag_ref[r] == 0)
            def _():
                pltpu.make_async_copy(table_ref.at[i], rows.at[slot, t], sems.at[slot]).start()

            @pl.when(lag_ref[r] != 0)
            def _():
                pltpu.make_async_copy(other_ref.at[i], rows.at[slot, t], sems.at[slot]).start()

            return carry

        lax.fori_loop(0, block, issue, 0, unroll=8)

    def wait(slot):
        def one_wait(t, carry):
            pltpu.make_async_copy(table_ref.at[0], rows.at[slot, t], sems.at[slot]).wait()
            return carry

        lax.fori_loop(0, block, one_wait, 0, unroll=8)

    slot = step % 2

    @pl.when(step == 0)
    def _():
        acc[...] = jnp.zeros_like(acc)
        fetch(0, 0)

    wait(slot)

    @pl.when(step + 1 < steps)
    def _():
        fetch(step + 1, 1 - slot)

    def one(t, carry):
        term = lax.dot_general(rows[slot, t], tiles_ref[t], (((1,), (1,)), ((), ())),
                               preferred_element_type=jnp.float32)
        o = obs_ref[step * block + t]
        acc[o] = acc[o] + term
        return carry

    lax.fori_loop(0, block, one, 0, unroll=32)

    @pl.when(step == steps - 1)
    def _():
        out_ref[...] = acc[: out_ref.shape[0]]


def field_partial(table, other, tile_index, tile_lag, tile_obs, tiles, observers):
    count, angles, width = table.shape
    n_tiles = tiles.shape[0]
    grid_spec = pltpu.PrefetchScalarGridSpec(
        num_scalar_prefetch=3,
        grid=(n_tiles // BLOCK,),
        in_specs=[
            pl.BlockSpec(memory_space=pl.ANY),
            pl.BlockSpec(memory_space=pl.ANY),
            pl.BlockSpec((BLOCK,) + tiles.shape[1:], lambda i, *_: (i, 0, 0)),
        ],
        out_specs=pl.BlockSpec((observers, angles, width), lambda i, *_: (0, 0, 0)),
        scratch_shapes=[
            pltpu.VMEM((2, BLOCK, angles, width), table.dtype),
            pltpu.VMEM((observers + 1, angles, width), jnp.float32),
            pltpu.SemaphoreType.DMA((2,)),
        ],
    )
    return pl.pallas_call(
        field_kernel,
        grid_spec=grid_spec,
        out_shape=jax.ShapeDtypeStruct((observers, angles, width), jnp.float32),
        compiler_params=pltpu.CompilerParams(dimension_semantics=("arbitrary",)),
    )(tile_index, tile_lag, tile_obs, table, other, tiles)


def shift_pairs(rows, cols, step, along_cols):
    pairs = []
    for a in range(rows):
        for b in range(cols):
            if along_cols:
                pairs.append((a * cols + b, a * cols + (b + step) % cols))
            else:
                pairs.append((a * cols + b, ((a + step) % rows) * cols + b))
    return pairs


def ring_gather(x, rows, cols, along_cols):
    n = cols if along_cols else rows
    assert n == 4
    n_lag = lax.axis_size("lag")
    plus = shift_pairs(rows, cols, 1, along_cols)
    minus = shift_pairs(rows, cols, -1, along_cols)
    from_behind = lax.ppermute(x, "grp", plus)
    from_ahead = lax.ppermute(x, "grp", minus)
    odd = lax.axis_index("lag") % 2 == 1
    send = jnp.where(odd, from_ahead, from_behind)
    pairs = []
    for l in range(n_lag):
        for src, dst in (minus if l % 2 else plus):
            pairs.append((src * n_lag + l, dst * n_lag + l))
    far = lax.ppermute(send, ("grp", "lag"), pairs)
    return jnp.stack([x, from_ahead, far, from_behind])

def body(history, tiles, tile_src, tile_obs, tile_lag, incident, near_inverse):
    n_grp = lax.axis_size("grp")
    n_lag = lax.axis_size("lag")
    obs_dev, ang_dev, width = incident.shape
    observers = obs_dev * n_grp
    hist16 = history.astype(jnp.bfloat16)
    lag_count, src_dev, angles, _ = hist16.shape
    rows = 4
    cols = n_grp // rows
    assert lag_count == 2 and rows * cols == n_grp
    table = ring_gather(ring_gather(hist16[0], rows, cols, True), rows, cols, False)
    table = table.reshape(n_grp * src_dev, angles, width)
    other = ring_gather(ring_gather(hist16[1], rows, cols, False), rows, cols, True)
    other = other.reshape(n_grp * src_dev, angles, width)
    me = lax.axis_index("grp")
    owner = tile_src // src_dev
    local = tile_src % src_dev
    dy = (owner // cols - me // cols + rows) % rows
    dz = (owner % cols - me % cols + cols) % cols
    tile_index = jnp.where(tile_lag == 0, (dy * cols + dz) * src_dev + local, (dz * rows + dy) * src_dev + local)
    partial = field_partial(table, other, tile_index, tile_lag, tile_obs, tiles, observers)
    partial = partial.reshape(n_grp, obs_dev, n_lag, ang_dev, width)
    partial = partial.transpose(0, 2, 1, 3, 4).reshape(n_grp * n_lag, obs_dev, ang_dev, width)
    received = lax.all_to_all(partial, ("grp", "lag"), 0, 0, tiled=True)
    field = jnp.sum(received, axis=0)
    rhs = (incident - field).astype(jnp.bfloat16)
    new_current = jnp.einsum("oag,ohg->oah", rhs, near_inverse, preferred_element_type=jnp.float32)
    return (field, new_current)


def solution(mesh):
    return jax.shard_map(
        body,
        mesh=mesh,
        in_specs=(
            P("lag", "grp", None, None),
            P(("grp", "lag"), None, None),
            P(("grp", "lag")),
            P(("grp", "lag")),
            P(("grp", "lag")),
            P("grp", "lag", None),
            P("grp", None, None),
        ),
        out_specs=(P("grp", "lag", None), P("grp", "lag", None)),
        check_vma=False,
    )
```

```python
import jax
import jax.numpy as jnp
from jax import lax
from jax.experimental import pallas as pl
from jax.experimental.pallas import tpu as pltpu
from jax.sharding import PartitionSpec as P

BLOCK = 128


def field_kernel(source_ref, index_ref, obs_ref, *refs):
    tables = refs[:-5]
    tiles_ref, out_ref, rows, acc, sems = refs[-5:]
    step = pl.program_id(0)
    steps = pl.num_programs(0)
    block = tiles_ref.shape[0]

    def fetch(which, slot):
        def issue(t, carry):
            r = which * block + t
            i = index_ref[r]
            k = source_ref[r]
            for j, table in enumerate(tables):
                @pl.when(k == j)
                def _():
                    pltpu.make_async_copy(table.at[i], rows.at[slot, t], sems.at[slot]).start()

            return carry

        lax.fori_loop(0, block, issue, 0, unroll=4)

    def wait(slot):
        def one_wait(t, carry):
            pltpu.make_async_copy(tables[0].at[0], rows.at[slot, t], sems.at[slot]).wait()
            return carry

        lax.fori_loop(0, block, one_wait, 0, unroll=8)

    slot = step % 2

    @pl.when(step == 0)
    def _():
        acc[...] = jnp.zeros_like(acc)
        fetch(0, 0)

    wait(slot)

    @pl.when(step + 1 < steps)
    def _():
        fetch(step + 1, 1 - slot)

    def one(t, carry):
        term = lax.dot_general(rows[slot, t], tiles_ref[t], (((1,), (1,)), ((), ())),
                               preferred_element_type=jnp.float32)
        o = obs_ref[step * block + t]
        acc[o] = acc[o] + term
        return carry

    lax.fori_loop(0, block, one, 0, unroll=32)

    @pl.when(step == steps - 1)
    def _():
        groups, lags, obs_dev, ang_dev, _ = out_ref.shape
        for g in range(groups):
            for l in range(lags):
                out_ref[g, l] = acc[g * obs_dev:(g + 1) * obs_dev, l * ang_dev:(l + 1) * ang_dev]


def field_partial(tables, source, tile_index, tile_obs, tiles, groups, lags, obs_dev):
    _, angles, width = tables[0].shape
    n_tiles = tiles.shape[0]
    ang_dev = angles // lags
    out_shape = (groups, lags, obs_dev, ang_dev, width)
    grid_spec = pltpu.PrefetchScalarGridSpec(
        num_scalar_prefetch=3,
        grid=(n_tiles // BLOCK,),
        in_specs=[pl.BlockSpec(memory_space=pl.ANY) for _ in tables] + [
            pl.BlockSpec((BLOCK,) + tiles.shape[1:], lambda i, *_: (i, 0, 0)),
        ],
        out_specs=pl.BlockSpec(out_shape, lambda i, *_: (0, 0, 0, 0, 0)),
        scratch_shapes=[
            pltpu.VMEM((2, BLOCK, angles, width), tables[0].dtype),
            pltpu.VMEM((groups * obs_dev + 1, angles, width), jnp.float32),
            pltpu.SemaphoreType.DMA((2,)),
        ],
    )
    return pl.pallas_call(
        field_kernel,
        grid_spec=grid_spec,
        out_shape=jax.ShapeDtypeStruct(out_shape, jnp.float32),
        compiler_params=pltpu.CompilerParams(dimension_semantics=("arbitrary",)),
    )(source, tile_index, tile_obs, *tables, tiles)


def shift_pairs(rows, cols, step, along_cols):
    pairs = []
    for a in range(rows):
        for b in range(cols):
            if along_cols:
                pairs.append((a * cols + b, a * cols + (b + step) % cols))
            else:
                pairs.append((a * cols + b, ((a + step) % rows) * cols + b))
    return pairs


def ring_gather(x, rows, cols, along_cols, pieces=False):
    n = cols if along_cols else rows
    plus = shift_pairs(rows, cols, 1, along_cols)
    minus = shift_pairs(rows, cols, -1, along_cols)
    from_behind = lax.ppermute(x, "grp", plus)
    from_ahead = lax.ppermute(x, "grp", minus)
    assert n == 4
    half = x.shape[0] // 2
    far_a = lax.ppermute(from_behind[:half], "grp", plus)
    far_b = lax.ppermute(from_ahead[half:], "grp", minus)
    if pieces:
        return [x, from_ahead, far_a, far_b, from_behind]
    far = jnp.concatenate([far_a, far_b], axis=0)
    return jnp.stack([x, from_ahead, far, from_behind])


def body(history, tiles, tile_src, tile_obs, tile_lag, incident, near_inverse):
    n_grp = lax.axis_size("grp")
    n_lag = lax.axis_size("lag")
    obs_dev, ang_dev, width = incident.shape
    observers = obs_dev * n_grp
    hist16 = history.astype(jnp.bfloat16)
    lag_count, src_dev, angles, _ = hist16.shape
    rows = 4
    cols = n_grp // rows
    assert lag_count == 2 and rows * cols == n_grp
    first = ring_gather(ring_gather(hist16[0], rows, cols, True), rows, cols, False, pieces=True)
    second = ring_gather(ring_gather(hist16[1], rows, cols, False), rows, cols, True, pieces=True)
    tables = [p.reshape(-1, angles, width) for p in first + second]
    me = lax.axis_index("grp")
    owner = tile_src // src_dev
    local = tile_src % src_dev
    dy = (owner // cols - me // cols + rows) % rows
    dz = (owner % cols - me % cols + cols) % cols
    outer = jnp.where(tile_lag == 0, dy, dz)
    inner = jnp.where(tile_lag == 0, dz, dy)
    upper = (outer == 2) & (inner >= 2)
    piece = jnp.where(outer == 3, 4, outer + upper.astype(outer.dtype))
    source = piece + 5 * tile_lag
    tile_index = (inner - 2 * upper.astype(inner.dtype)) * src_dev + local
    partial = field_partial(tables, source, tile_index, tile_obs, tiles, n_grp, n_lag, obs_dev)
    partial = partial.reshape(n_grp * n_lag, obs_dev, ang_dev, width)
    received = lax.all_to_all(partial, ("grp", "lag"), 0, 0, tiled=True)
    field = jnp.sum(received, axis=0)
    rhs = (incident - field).astype(jnp.bfloat16)
    new_current = jnp.einsum("oag,ohg->oah", rhs, near_inverse, preferred_element_type=jnp.float32)
    return (field, new_current)


def solution(mesh):
    return jax.shard_map(
        body,
        mesh=mesh,
        in_specs=(
            P("lag", "grp", None, None),
            P(("grp", "lag"), None, None),
            P(("grp", "lag")),
            P(("grp", "lag")),
            P(("grp", "lag")),
            P("grp", "lag", None),
            P("grp", None, None),
        ),
        out_specs=(P("grp", "lag", None), P("grp", "lag", None)),
        check_vma=False,
    )
```

```python
import jax
import jax.numpy as jnp
from jax import lax
from jax.experimental import pallas as pl
from jax.experimental.pallas import tpu as pltpu
from jax.sharding import PartitionSpec as P

BLOCK = 128


def field_kernel(source_ref, index_ref, obs_ref, *refs):
    tables = refs[:-5]
    tiles_ref, out_ref, rows, acc, sems = refs[-5:]
    step = pl.program_id(0)
    steps = pl.num_programs(0)
    block = tiles_ref.shape[0]

    def fetch(which, slot):
        def issue(t, carry):
            r = which * block + t
            i = index_ref[r]
            k = source_ref[r]
            for j, table in enumerate(tables):
                @pl.when(k == j)
                def _():
                    pltpu.make_async_copy(table.at[i], rows.at[slot, t], sems.at[slot]).start()

            return carry

        lax.fori_loop(0, block, issue, 0, unroll=4)

    def wait(slot):
        def one_wait(t, carry):
            pltpu.make_async_copy(tables[0].at[0], rows.at[slot, t], sems.at[slot]).wait()
            return carry

        lax.fori_loop(0, block, one_wait, 0, unroll=8)

    slot = step % 2

    @pl.when(step == 0)
    def _():
        acc[...] = jnp.zeros_like(acc)
        fetch(0, 0)

    wait(slot)

    @pl.when(step + 1 < steps)
    def _():
        fetch(step + 1, 1 - slot)

    def one(t, carry):
        term = lax.dot_general(rows[slot, t], tiles_ref[t], (((1,), (1,)), ((), ())),
                               preferred_element_type=jnp.float32)
        o = obs_ref[step * block + t]
        acc[o] = acc[o] + term
        return carry

    lax.fori_loop(0, block, one, 0, unroll=32)

    @pl.when(step == steps - 1)
    def _():
        groups, lags, obs_dev, ang_dev, _ = out_ref.shape
        for g in range(groups):
            for l in range(lags):
                out_ref[g, l] = acc[g * obs_dev:(g + 1) * obs_dev, l * ang_dev:(l + 1) * ang_dev]


def field_partial(tables, source, tile_index, tile_obs, tiles, groups, lags, obs_dev):
    _, angles, width = tables[0].shape
    n_tiles = tiles.shape[0]
    ang_dev = angles // lags
    out_shape = (groups, lags, obs_dev, ang_dev, width)
    grid_spec = pltpu.PrefetchScalarGridSpec(
        num_scalar_prefetch=3,
        grid=(n_tiles // BLOCK,),
        in_specs=[pl.BlockSpec(memory_space=pl.ANY) for _ in tables] + [
            pl.BlockSpec((BLOCK,) + tiles.shape[1:], lambda i, *_: (i, 0, 0)),
        ],
        out_specs=pl.BlockSpec(out_shape, lambda i, *_: (0, 0, 0, 0, 0)),
        scratch_shapes=[
            pltpu.VMEM((2, BLOCK, angles, width), tables[0].dtype),
            pltpu.VMEM((groups * obs_dev + 1, angles, width), jnp.float32),
            pltpu.SemaphoreType.DMA((2,)),
        ],
    )
    return pl.pallas_call(
        field_kernel,
        grid_spec=grid_spec,
        out_shape=jax.ShapeDtypeStruct(out_shape, jnp.float32),
        compiler_params=pltpu.CompilerParams(dimension_semantics=("arbitrary",)),
    )(source, tile_index, tile_obs, *tables, tiles)


def shift_pairs(rows, cols, step, along_cols):
    pairs = []
    for a in range(rows):
        for b in range(cols):
            if along_cols:
                pairs.append((a * cols + b, a * cols + (b + step) % cols))
            else:
                pairs.append((a * cols + b, ((a + step) % rows) * cols + b))
    return pairs


def ring_gather(x, rows, cols, along_cols, pieces=False, direct=False):
    n = cols if along_cols else rows
    plus = shift_pairs(rows, cols, 1, along_cols)
    minus = shift_pairs(rows, cols, -1, along_cols)
    from_behind = lax.ppermute(x, "grp", plus)
    from_ahead = lax.ppermute(x, "grp", minus)
    assert n == 4
    if direct:
        far = lax.ppermute(x, "grp", shift_pairs(rows, cols, 2, along_cols))
        return jnp.stack([x, from_ahead, far, from_behind])
    half = x.shape[0] // 2
    far_a = lax.ppermute(from_behind[:half], "grp", plus)
    far_b = lax.ppermute(from_ahead[half:], "grp", minus)
    if pieces:
        return [x, from_ahead, far_a, far_b, from_behind]
    far = jnp.concatenate([far_a, far_b], axis=0)
    return jnp.stack([x, from_ahead, far, from_behind])


def body(history, tiles, tile_src, tile_obs, tile_lag, incident, near_inverse):
    n_grp = lax.axis_size("grp")
    n_lag = lax.axis_size("lag")
    obs_dev, ang_dev, width = incident.shape
    observers = obs_dev * n_grp
    hist16 = history.astype(jnp.bfloat16)
    lag_count, src_dev, angles, _ = hist16.shape
    rows = 4
    cols = n_grp // rows
    assert lag_count == 2 and rows * cols == n_grp
    first = ring_gather(ring_gather(hist16[0], rows, cols, True, direct=True), rows, cols, False, pieces=True)
    second = ring_gather(ring_gather(hist16[1], rows, cols, False, direct=True), rows, cols, True, pieces=True)
    tables = [p.reshape(-1, angles, width) for p in first + second]
    me = lax.axis_index("grp")
    owner = tile_src // src_dev
    local = tile_src % src_dev
    dy = (owner // cols - me // cols + rows) % rows
    dz = (owner % cols - me % cols + cols) % cols
    outer = jnp.where(tile_lag == 0, dy, dz)
    inner = jnp.where(tile_lag == 0, dz, dy)
    upper = (outer == 2) & (inner >= 2)
    piece = jnp.where(outer == 3, 4, outer + upper.astype(outer.dtype))
    source = piece + 5 * tile_lag
    tile_index = (inner - 2 * upper.astype(inner.dtype)) * src_dev + local
    partial = field_partial(tables, source, tile_index, tile_obs, tiles, n_grp, n_lag, obs_dev)
    partial = partial.reshape(n_grp * n_lag, obs_dev, ang_dev, width)
    received = lax.all_to_all(partial, ("grp", "lag"), 0, 0, tiled=True)
    field = jnp.sum(received, axis=0)
    rhs = (incident - field).astype(jnp.bfloat16)
    new_current = jnp.einsum("oag,ohg->oah", rhs, near_inverse, preferred_element_type=jnp.float32)
    return (field, new_current)


def solution(mesh):
    return jax.shard_map(
        body,
        mesh=mesh,
        in_specs=(
            P("lag", "grp", None, None),
            P(("grp", "lag"), None, None),
            P(("grp", "lag")),
            P(("grp", "lag")),
            P(("grp", "lag")),
            P("grp", "lag", None),
            P("grp", None, None),
        ),
        out_specs=(P("grp", "lag", None), P("grp", "lag", None)),
        check_vma=False,
    )
```

```python
import jax
import jax.numpy as jnp
from jax import lax
from jax.experimental import pallas as pl
from jax.experimental.pallas import tpu as pltpu
from jax.sharding import PartitionSpec as P

BLOCK = 128


def field_kernel(index_ref, obs_ref, *refs):
    pieces = refs[:-5]
    tiles_ref, out_ref, table, acc, sems = refs[-5:]
    step = pl.program_id(0)
    steps = pl.num_programs(0)
    block = tiles_ref.shape[0]

    @pl.when(step == 0)
    def _():
        copies = []
        offset = 0
        for j, piece in enumerate(pieces):
            size = piece.shape[0]
            copy = pltpu.make_async_copy(piece, table.at[pl.ds(offset, size)], sems.at[j])
            copy.start()
            copies.append(copy)
            offset += size
        acc[...] = jnp.zeros_like(acc)
        for copy in copies:
            copy.wait()

    def one(t, carry):
        r = step * block + t
        term = lax.dot_general(table[index_ref[r]], tiles_ref[t], (((1,), (1,)), ((), ())),
                               preferred_element_type=jnp.float32)
        o = obs_ref[r]
        acc[o] = acc[o] + term
        return carry

    lax.fori_loop(0, block, one, 0, unroll=32)

    @pl.when(step == steps - 1)
    def _():
        groups, lags, obs_dev, ang_dev, _ = out_ref.shape
        for g in range(groups):
            for l in range(lags):
                out_ref[g, l] = acc[g * obs_dev:(g + 1) * obs_dev, l * ang_dev:(l + 1) * ang_dev]


def field_partial(pieces, tile_index, tile_obs, tiles, groups, lags, obs_dev):
    _, angles, width = pieces[0].shape
    total = sum(piece.shape[0] for piece in pieces)
    n_tiles = tiles.shape[0]
    ang_dev = angles // lags
    out_shape = (groups, lags, obs_dev, ang_dev, width)
    grid_spec = pltpu.PrefetchScalarGridSpec(
        num_scalar_prefetch=2,
        grid=(n_tiles // BLOCK,),
        in_specs=[pl.BlockSpec(memory_space=pl.ANY) for _ in pieces] + [
            pl.BlockSpec((BLOCK,) + tiles.shape[1:], lambda i, *_: (i, 0, 0)),
        ],
        out_specs=pl.BlockSpec(out_shape, lambda i, *_: (0, 0, 0, 0, 0)),
        scratch_shapes=[
            pltpu.VMEM((total, angles, width), pieces[0].dtype),
            pltpu.VMEM((groups * obs_dev + 1, angles, width), jnp.float32),
            pltpu.SemaphoreType.DMA((len(pieces),)),
        ],
    )
    return pl.pallas_call(
        field_kernel,
        grid_spec=grid_spec,
        out_shape=jax.ShapeDtypeStruct(out_shape, jnp.float32),
        compiler_params=pltpu.CompilerParams(dimension_semantics=("arbitrary",)),
    )(tile_index, tile_obs, *pieces, tiles)


def shift_pairs(rows, cols, step, along_cols):
    pairs = []
    for a in range(rows):
        for b in range(cols):
            if along_cols:
                pairs.append((a * cols + b, a * cols + (b + step) % cols))
            else:
                pairs.append((a * cols + b, ((a + step) % rows) * cols + b))
    return pairs


def ring_gather(x, rows, cols, along_cols, pieces=False):
    n = cols if along_cols else rows
    plus = shift_pairs(rows, cols, 1, along_cols)
    minus = shift_pairs(rows, cols, -1, along_cols)
    from_behind = lax.ppermute(x, "grp", plus)
    from_ahead = lax.ppermute(x, "grp", minus)
    assert n == 4
    half = x.shape[0] // 2
    far_a = lax.ppermute(from_behind[:half], "grp", plus)
    far_b = lax.ppermute(from_ahead[half:], "grp", minus)
    if pieces:
        return [x, from_ahead, far_a, far_b, from_behind]
    far = jnp.concatenate([far_a, far_b], axis=0)
    return jnp.stack([x, from_ahead, far, from_behind])


def body(history, tiles, tile_src, tile_obs, tile_lag, incident, near_inverse):
    n_grp = lax.axis_size("grp")
    n_lag = lax.axis_size("lag")
    obs_dev, ang_dev, width = incident.shape
    observers = obs_dev * n_grp
    hist16 = history.astype(jnp.bfloat16)
    lag_count, src_dev, angles, _ = hist16.shape
    rows = 4
    cols = n_grp // rows
    assert lag_count == 2 and rows * cols == n_grp
    first = ring_gather(ring_gather(hist16[0], rows, cols, True), rows, cols, False, pieces=True)
    second = ring_gather(ring_gather(hist16[1], rows, cols, False), rows, cols, True, pieces=True)
    tables = [p.reshape(-1, angles, width) for p in first + second]
    me = lax.axis_index("grp")
    owner = tile_src // src_dev
    local = tile_src % src_dev
    dy = (owner // cols - me // cols + rows) % rows
    dz = (owner % cols - me % cols + cols) % cols
    outer = jnp.where(tile_lag == 0, dy, dz)
    inner = jnp.where(tile_lag == 0, dz, dy)
    upper = (outer == 2) & (inner >= 2)
    piece = jnp.where(outer == 3, 4, outer + upper.astype(outer.dtype))
    source = piece + 5 * tile_lag
    starts = [0]
    for table in tables[:-1]:
        starts.append(starts[-1] + table.shape[0])
    start = jnp.asarray(starts, jnp.int32)[source]
    tile_index = start + (inner - 2 * upper.astype(inner.dtype)) * src_dev + local
    partial = field_partial(tables, tile_index, tile_obs, tiles, n_grp, n_lag, obs_dev)
    partial = partial.reshape(n_grp * n_lag, obs_dev, ang_dev, width)
    received = lax.all_to_all(partial, ("grp", "lag"), 0, 0, tiled=True)
    field = jnp.sum(received, axis=0)
    rhs = (incident - field).astype(jnp.bfloat16)
    new_current = jnp.einsum("oag,ohg->oah", rhs, near_inverse, preferred_element_type=jnp.float32)
    return (field, new_current)


def solution(mesh):
    return jax.shard_map(
        body,
        mesh=mesh,
        in_specs=(
            P("lag", "grp", None, None),
            P(("grp", "lag"), None, None),
            P(("grp", "lag")),
            P(("grp", "lag")),
            P(("grp", "lag")),
            P("grp", "lag", None),
            P("grp", None, None),
        ),
        out_specs=(P("grp", "lag", None), P("grp", "lag", None)),
        check_vma=False,
    )
```

```python
import jax
import jax.numpy as jnp
from jax import lax
from jax.experimental import pallas as pl
from jax.experimental.pallas import tpu as pltpu
from jax.sharding import PartitionSpec as P

BLOCK = 128


def field_kernel(index_ref, obs_ref, *refs):
    pieces = refs[:-5]
    tiles_ref, out_ref, table, acc, sems = refs[-5:]
    step = pl.program_id(0)
    steps = pl.num_programs(0)
    block = tiles_ref.shape[0]

    @pl.when(step == 0)
    def _():
        copies = []
        offset = 0
        for j, piece in enumerate(pieces):
            size = piece.shape[0]
            copy = pltpu.make_async_copy(piece, table.at[pl.ds(offset, size)], sems.at[j])
            copy.start()
            copies.append(copy)
            offset += size
        acc[...] = jnp.zeros_like(acc)
        for copy in copies:
            copy.wait()

    def one(t, carry):
        r = step * block + t
        term = lax.dot_general(table[index_ref[r]], tiles_ref[t], (((1,), (1,)), ((), ())),
                               preferred_element_type=jnp.float32)
        o = obs_ref[r]
        acc[o] = acc[o] + term
        return carry

    lax.fori_loop(0, block, one, 0, unroll=32)

    @pl.when(step == steps - 1)
    def _():
        lags, groups, obs_dev, ang_dev, _ = out_ref.shape
        for g in range(groups):
            for l in range(lags):
                out_ref[l, g] = acc[g * obs_dev:(g + 1) * obs_dev, l * ang_dev:(l + 1) * ang_dev]


def field_partial(pieces, tile_index, tile_obs, tiles, groups, lags, obs_dev):
    _, angles, width = pieces[0].shape
    total = sum(piece.shape[0] for piece in pieces)
    n_tiles = tiles.shape[0]
    ang_dev = angles // lags
    out_shape = (lags, groups, obs_dev, ang_dev, width)
    grid_spec = pltpu.PrefetchScalarGridSpec(
        num_scalar_prefetch=2,
        grid=(n_tiles // BLOCK,),
        in_specs=[pl.BlockSpec(memory_space=pl.ANY) for _ in pieces] + [
            pl.BlockSpec((BLOCK,) + tiles.shape[1:], lambda i, *_: (i, 0, 0)),
        ],
        out_specs=pl.BlockSpec(out_shape, lambda i, *_: (0, 0, 0, 0, 0)),
        scratch_shapes=[
            pltpu.VMEM((total, angles, width), pieces[0].dtype),
            pltpu.VMEM((groups * obs_dev + 1, angles, width), jnp.float32),
            pltpu.SemaphoreType.DMA((len(pieces),)),
        ],
    )
    return pl.pallas_call(
        field_kernel,
        grid_spec=grid_spec,
        out_shape=jax.ShapeDtypeStruct(out_shape, jnp.float32),
        compiler_params=pltpu.CompilerParams(dimension_semantics=("arbitrary",)),
    )(tile_index, tile_obs, *pieces, tiles)


def shift_pairs(rows, cols, step, along_cols):
    pairs = []
    for a in range(rows):
        for b in range(cols):
            if along_cols:
                pairs.append((a * cols + b, a * cols + (b + step) % cols))
            else:
                pairs.append((a * cols + b, ((a + step) % rows) * cols + b))
    return pairs


def ring_gather(x, rows, cols, along_cols, pieces=False):
    n = cols if along_cols else rows
    plus = shift_pairs(rows, cols, 1, along_cols)
    minus = shift_pairs(rows, cols, -1, along_cols)
    from_behind = lax.ppermute(x, "grp", plus)
    from_ahead = lax.ppermute(x, "grp", minus)
    assert n == 4
    half = x.shape[0] // 2
    far_a = lax.ppermute(from_behind[:half], "grp", plus)
    far_b = lax.ppermute(from_ahead[half:], "grp", minus)
    if pieces:
        return [x, from_ahead, far_a, far_b, from_behind]
    far = jnp.concatenate([far_a, far_b], axis=0)
    return jnp.stack([x, from_ahead, far, from_behind])


def body(history, tiles, tile_src, tile_obs, tile_lag, incident, near_inverse):
    n_grp = lax.axis_size("grp")
    n_lag = lax.axis_size("lag")
    obs_dev, ang_dev, width = incident.shape
    observers = obs_dev * n_grp
    hist16 = history.astype(jnp.bfloat16)
    lag_count, src_dev, angles, _ = hist16.shape
    rows = 4
    cols = n_grp // rows
    assert lag_count == 2 and rows * cols == n_grp
    first = ring_gather(ring_gather(hist16[0], rows, cols, True), rows, cols, False, pieces=True)
    second = ring_gather(ring_gather(hist16[1], rows, cols, False), rows, cols, True, pieces=True)
    tables = [p.reshape(-1, angles, width) for p in first + second]
    me = lax.axis_index("grp")
    owner = tile_src // src_dev
    local = tile_src % src_dev
    dy = (owner // cols - me // cols + rows) % rows
    dz = (owner % cols - me % cols + cols) % cols
    outer = jnp.where(tile_lag == 0, dy, dz)
    inner = jnp.where(tile_lag == 0, dz, dy)
    upper = (outer == 2) & (inner >= 2)
    piece = jnp.where(outer == 3, 4, outer + upper.astype(outer.dtype))
    source = piece + 5 * tile_lag
    starts = [0]
    for table in tables[:-1]:
        starts.append(starts[-1] + table.shape[0])
    start = jnp.asarray(starts, jnp.int32)[source]
    tile_index = start + (inner - 2 * upper.astype(inner.dtype)) * src_dev + local
    partial = field_partial(tables, tile_index, tile_obs, tiles, n_grp, n_lag, obs_dev)
    partial = partial.reshape(n_grp * n_lag, obs_dev, ang_dev, width)
    received = lax.all_to_all(partial, ("lag", "grp"), 0, 0, tiled=True)
    field = jnp.sum(received, axis=0)
    rhs = (incident - field).astype(jnp.bfloat16)
    new_current = jnp.einsum("oag,ohg->oah", rhs, near_inverse, preferred_element_type=jnp.float32)
    return (field, new_current)


def solution(mesh):
    return jax.shard_map(
        body,
        mesh=mesh,
        in_specs=(
            P("lag", "grp", None, None),
            P(("grp", "lag"), None, None),
            P(("grp", "lag")),
            P(("grp", "lag")),
            P(("grp", "lag")),
            P("grp", "lag", None),
            P("grp", None, None),
        ),
        out_specs=(P("grp", "lag", None), P("grp", "lag", None)),
        check_vma=False,
    )
```

```python
import jax
import jax.numpy as jnp
from jax import lax
from jax.experimental import pallas as pl
from jax.experimental.pallas import tpu as pltpu
from jax.sharding import PartitionSpec as P

BLOCK = 128


def field_kernel(index_ref, obs_ref, *refs):
    pieces = refs[:-5]
    tiles_ref, out_ref, table, acc, sems = refs[-5:]
    step = pl.program_id(0)
    steps = pl.num_programs(0)
    block = tiles_ref.shape[0]

    @pl.when(step == 0)
    def _():
        copies = []
        offset = 0
        for j, piece in enumerate(pieces):
            size = piece.shape[0]
            copy = pltpu.make_async_copy(piece, table.at[pl.ds(offset, size)], sems.at[j])
            copy.start()
            copies.append(copy)
            offset += size
        acc[...] = jnp.zeros_like(acc)
        for copy in copies:
            copy.wait()

    def one(t, carry):
        r = step * block + t
        term = lax.dot_general(table[index_ref[r]], tiles_ref[t], (((1,), (1,)), ((), ())),
                               preferred_element_type=jnp.float32)
        o = obs_ref[r]
        acc[o] = acc[o] + term
        return carry

    lax.fori_loop(0, block, one, 0, unroll=32)

    @pl.when(step == steps - 1)
    def _():
        lags, groups, obs_dev, ang_dev, _ = out_ref.shape
        for g in range(groups):
            for l in range(lags):
                out_ref[l, g] = acc[g * obs_dev:(g + 1) * obs_dev, l * ang_dev:(l + 1) * ang_dev]


def field_partial(pieces, tile_index, tile_obs, tiles, groups, lags, obs_dev):
    _, angles, width = pieces[0].shape
    total = sum(piece.shape[0] for piece in pieces)
    n_tiles = tiles.shape[0]
    ang_dev = angles // lags
    out_shape = (lags, groups, obs_dev, ang_dev, width)
    grid_spec = pltpu.PrefetchScalarGridSpec(
        num_scalar_prefetch=2,
        grid=(n_tiles // BLOCK,),
        in_specs=[pl.BlockSpec(memory_space=pl.ANY) for _ in pieces] + [
            pl.BlockSpec((BLOCK,) + tiles.shape[1:], lambda i, *_: (i, 0, 0)),
        ],
        out_specs=pl.BlockSpec(out_shape, lambda i, *_: (0, 0, 0, 0, 0)),
        scratch_shapes=[
            pltpu.VMEM((total, angles, width), pieces[0].dtype),
            pltpu.VMEM((groups * obs_dev + 1, angles, width), jnp.float32),
            pltpu.SemaphoreType.DMA((len(pieces),)),
        ],
    )
    return pl.pallas_call(
        field_kernel,
        grid_spec=grid_spec,
        out_shape=jax.ShapeDtypeStruct(out_shape, jnp.float32),
        compiler_params=pltpu.CompilerParams(dimension_semantics=("arbitrary",)),
    )(tile_index, tile_obs, *pieces, tiles)


def shift_pairs(rows, cols, step, along_cols):
    pairs = []
    for a in range(rows):
        for b in range(cols):
            if along_cols:
                pairs.append((a * cols + b, a * cols + (b + step) % cols))
            else:
                pairs.append((a * cols + b, ((a + step) % rows) * cols + b))
    return pairs


def ring_gather(x, rows, cols, along_cols, pieces=False):
    n = cols if along_cols else rows
    plus = shift_pairs(rows, cols, 1, along_cols)
    minus = shift_pairs(rows, cols, -1, along_cols)
    from_behind = lax.ppermute(x, "grp", plus)
    from_ahead = lax.ppermute(x, "grp", minus)
    assert n == 4
    half = x.shape[0] // 2
    far_a = lax.ppermute(from_behind[:half], "grp", plus)
    far_b = lax.ppermute(from_ahead[half:], "grp", minus)
    if pieces:
        return [x, from_ahead, far_a, far_b, from_behind]
    far = jnp.concatenate([far_a, far_b], axis=0)
    return jnp.stack([x, from_ahead, far, from_behind])


def body(history, tiles, tile_src, tile_obs, tile_lag, incident, near_inverse):
    n_grp = lax.axis_size("grp")
    n_lag = lax.axis_size("lag")
    obs_dev, ang_dev, width = incident.shape
    observers = obs_dev * n_grp
    lag_count, src_dev, angles, _ = history.shape
    rows = 4
    cols = n_grp // rows
    assert lag_count == 2 and rows * cols == n_grp
    first = ring_gather(ring_gather(history[0].astype(jnp.bfloat16), rows, cols, True), rows, cols, False, pieces=True)
    second = ring_gather(ring_gather(history[1].astype(jnp.bfloat16), rows, cols, False), rows, cols, True, pieces=True)
    tables = [p.reshape(-1, angles, width) for p in first + second]
    me = lax.axis_index("grp")
    owner = tile_src // src_dev
    local = tile_src % src_dev
    dy = (owner // cols - me // cols + rows) % rows
    dz = (owner % cols - me % cols + cols) % cols
    outer = jnp.where(tile_lag == 0, dy, dz)
    inner = jnp.where(tile_lag == 0, dz, dy)
    upper = (outer == 2) & (inner >= 2)
    piece = jnp.where(outer == 3, 4, outer + upper.astype(outer.dtype))
    source = piece + 5 * tile_lag
    starts = [0]
    for table in tables[:-1]:
        starts.append(starts[-1] + table.shape[0])
    start = jnp.asarray(starts, jnp.int32)[source]
    tile_index = start + (inner - 2 * upper.astype(inner.dtype)) * src_dev + local
    partial = field_partial(tables, tile_index, tile_obs, tiles, n_grp, n_lag, obs_dev)
    partial = partial.reshape(n_grp * n_lag, obs_dev, ang_dev, width)
    received = lax.all_to_all(partial, ("lag", "grp"), 0, 0, tiled=True)
    field = jnp.sum(received, axis=0)
    rhs = (incident - field).astype(jnp.bfloat16)
    new_current = jnp.einsum("oag,ohg->oah", rhs, near_inverse, preferred_element_type=jnp.float32)
    return (field, new_current)


def solution(mesh):
    return jax.shard_map(
        body,
        mesh=mesh,
        in_specs=(
            P("lag", "grp", None, None),
            P(("grp", "lag"), None, None),
            P(("grp", "lag")),
            P(("grp", "lag")),
            P(("grp", "lag")),
            P("grp", "lag", None),
            P("grp", None, None),
        ),
        out_specs=(P("grp", "lag", None), P("grp", "lag", None)),
        check_vma=False,
    )
```

```python
import jax
import jax.numpy as jnp
from jax import lax
from jax.experimental import pallas as pl
from jax.experimental.pallas import tpu as pltpu
from jax.sharding import PartitionSpec as P

BLOCK = 128


def field_kernel(index_ref, obs_ref, *refs):
    pieces = refs[:-6]
    tiles_hbm, out_ref, table, tiles_ref, acc, sems = refs[-6:]
    step = pl.program_id(0)
    steps = pl.num_programs(0)
    block = tiles_ref.shape[1]
    slot = step % 2

    def tiles_copy(which, into):
        return pltpu.make_async_copy(tiles_hbm.at[pl.ds(which * block, block)], tiles_ref.at[into], sems.at[len(pieces) + into])

    @pl.when(step == 0)
    def _():
        tiles_copy(0, 0).start()
        copies = []
        offset = 0
        for j, piece in enumerate(pieces):
            size = piece.shape[0]
            copy = pltpu.make_async_copy(piece, table.at[pl.ds(offset, size)], sems.at[j])
            copy.start()
            copies.append(copy)
            offset += size
        acc[...] = jnp.zeros_like(acc)
        for copy in copies:
            copy.wait()

    tiles_copy(step, slot).wait()

    @pl.when(step + 1 < steps)
    def _():
        tiles_copy(step + 1, 1 - slot).start()

    def one(t, carry):
        r = step * block + t
        term = lax.dot_general(table[index_ref[r]], tiles_ref[slot, t], (((1,), (1,)), ((), ())),
                               preferred_element_type=jnp.float32)
        o = obs_ref[r]
        acc[o] = acc[o] + term
        return carry

    lax.fori_loop(0, block, one, 0, unroll=32)

    @pl.when(step == steps - 1)
    def _():
        lags, groups, obs_dev, ang_dev, _ = out_ref.shape
        for g in range(groups):
            for l in range(lags):
                out_ref[l, g] = acc[g * obs_dev:(g + 1) * obs_dev, l * ang_dev:(l + 1) * ang_dev]


def field_partial(pieces, tile_index, tile_obs, tiles, groups, lags, obs_dev):
    _, angles, width = pieces[0].shape
    total = sum(piece.shape[0] for piece in pieces)
    n_tiles = tiles.shape[0]
    ang_dev = angles // lags
    out_shape = (lags, groups, obs_dev, ang_dev, width)
    grid_spec = pltpu.PrefetchScalarGridSpec(
        num_scalar_prefetch=2,
        grid=(n_tiles // BLOCK,),
        in_specs=[pl.BlockSpec(memory_space=pl.ANY) for _ in pieces] + [pl.BlockSpec(memory_space=pl.ANY)],
        out_specs=pl.BlockSpec(out_shape, lambda i, *_: (0, 0, 0, 0, 0)),
        scratch_shapes=[
            pltpu.VMEM((total, angles, width), pieces[0].dtype),
            pltpu.VMEM((2, BLOCK) + tiles.shape[1:], tiles.dtype),
            pltpu.VMEM((groups * obs_dev + 1, angles, width), jnp.float32),
            pltpu.SemaphoreType.DMA((len(pieces) + 2,)),
        ],
    )
    return pl.pallas_call(
        field_kernel,
        grid_spec=grid_spec,
        out_shape=jax.ShapeDtypeStruct(out_shape, jnp.float32),
        compiler_params=pltpu.CompilerParams(dimension_semantics=("arbitrary",)),
    )(tile_index, tile_obs, *pieces, tiles)


def shift_pairs(rows, cols, step, along_cols):
    pairs = []
    for a in range(rows):
        for b in range(cols):
            if along_cols:
                pairs.append((a * cols + b, a * cols + (b + step) % cols))
            else:
                pairs.append((a * cols + b, ((a + step) % rows) * cols + b))
    return pairs


def ring_gather(x, rows, cols, along_cols, pieces=False):
    n = cols if along_cols else rows
    plus = shift_pairs(rows, cols, 1, along_cols)
    minus = shift_pairs(rows, cols, -1, along_cols)
    from_behind = lax.ppermute(x, "grp", plus)
    from_ahead = lax.ppermute(x, "grp", minus)
    assert n == 4
    half = x.shape[0] // 2
    far_a = lax.ppermute(from_behind[:half], "grp", plus)
    far_b = lax.ppermute(from_ahead[half:], "grp", minus)
    if pieces:
        return [x, from_ahead, far_a, far_b, from_behind]
    far = jnp.concatenate([far_a, far_b], axis=0)
    return jnp.stack([x, from_ahead, far, from_behind])


def body(history, tiles, tile_src, tile_obs, tile_lag, incident, near_inverse):
    n_grp = lax.axis_size("grp")
    n_lag = lax.axis_size("lag")
    obs_dev, ang_dev, width = incident.shape
    observers = obs_dev * n_grp
    lag_count, src_dev, angles, _ = history.shape
    rows = 4
    cols = n_grp // rows
    assert lag_count == 2 and rows * cols == n_grp
    first = ring_gather(ring_gather(history[0].astype(jnp.bfloat16), rows, cols, True), rows, cols, False, pieces=True)
    second = ring_gather(ring_gather(history[1].astype(jnp.bfloat16), rows, cols, False), rows, cols, True, pieces=True)
    tables = [p.reshape(-1, angles, width) for p in first + second]
    me = lax.axis_index("grp")
    owner = tile_src // src_dev
    local = tile_src % src_dev
    dy = (owner // cols - me // cols + rows) % rows
    dz = (owner % cols - me % cols + cols) % cols
    outer = jnp.where(tile_lag == 0, dy, dz)
    inner = jnp.where(tile_lag == 0, dz, dy)
    upper = (outer == 2) & (inner >= 2)
    piece = jnp.where(outer == 3, 4, outer + upper.astype(outer.dtype))
    source = piece + 5 * tile_lag
    starts = [0]
    for table in tables[:-1]:
        starts.append(starts[-1] + table.shape[0])
    start = jnp.asarray(starts, jnp.int32)[source]
    tile_index = start + (inner - 2 * upper.astype(inner.dtype)) * src_dev + local
    partial = field_partial(tables, tile_index, tile_obs, tiles, n_grp, n_lag, obs_dev)
    partial = partial.reshape(n_grp * n_lag, obs_dev, ang_dev, width)
    received = lax.all_to_all(partial, ("lag", "grp"), 0, 0, tiled=True)
    field = jnp.sum(received, axis=0)
    rhs = (incident - field).astype(jnp.bfloat16)
    new_current = jnp.einsum("oag,ohg->oah", rhs, near_inverse, preferred_element_type=jnp.float32)
    return (field, new_current)


def solution(mesh):
    return jax.shard_map(
        body,
        mesh=mesh,
        in_specs=(
            P("lag", "grp", None, None),
            P(("grp", "lag"), None, None),
            P(("grp", "lag")),
            P(("grp", "lag")),
            P(("grp", "lag")),
            P("grp", "lag", None),
            P("grp", None, None),
        ),
        out_specs=(P("grp", "lag", None), P("grp", "lag", None)),
        check_vma=False,
    )
```

```python
import jax
import jax.numpy as jnp
from jax import lax
from jax.experimental import pallas as pl
from jax.experimental.pallas import tpu as pltpu
from jax.sharding import PartitionSpec as P

BLOCK = 128


def field_kernel(index_ref, obs_ref, *refs):
    pieces = refs[:-6]
    tiles_hbm, out_ref, table, tiles_ref, acc, sems = refs[-6:]
    step = pl.program_id(0)
    steps = pl.num_programs(0)
    block = tiles_ref.shape[1]
    slot = step % 2

    def tiles_copy(which, into):
        return pltpu.make_async_copy(tiles_hbm.at[pl.ds(which * block, block)], tiles_ref.at[into], sems.at[len(pieces) + into])

    @pl.when(step == 0)
    def _():
        tiles_copy(0, 0).start()
        copies = []
        offset = 0
        for j, piece in enumerate(pieces):
            size = piece.shape[0]
            copy = pltpu.make_async_copy(piece, table.at[pl.ds(offset, size)], sems.at[j])
            copy.start()
            copies.append(copy)
            offset += size
        acc[...] = jnp.zeros_like(acc)
        for copy in copies:
            copy.wait()

    tiles_copy(step, slot).wait()

    @pl.when(step + 1 < steps)
    def _():
        tiles_copy(step + 1, 1 - slot).start()

    def one(t, carry):
        r = step * block + t
        term = lax.dot_general(table[index_ref[r]], tiles_ref[slot, t], (((1,), (1,)), ((), ())),
                               preferred_element_type=jnp.float32)
        o = obs_ref[r]
        acc[o] = acc[o] + term
        return carry

    lax.fori_loop(0, block, one, 0, unroll=block)

    @pl.when(step == steps - 1)
    def _():
        lags, groups, obs_dev, ang_dev, _ = out_ref.shape
        for g in range(groups):
            for l in range(lags):
                out_ref[l, g] = acc[g * obs_dev:(g + 1) * obs_dev, l * ang_dev:(l + 1) * ang_dev]


def field_partial(pieces, tile_index, tile_obs, tiles, groups, lags, obs_dev):
    _, angles, width = pieces[0].shape
    total = sum(piece.shape[0] for piece in pieces)
    n_tiles = tiles.shape[0]
    ang_dev = angles // lags
    out_shape = (lags, groups, obs_dev, ang_dev, width)
    grid_spec = pltpu.PrefetchScalarGridSpec(
        num_scalar_prefetch=2,
        grid=(n_tiles // BLOCK,),
        in_specs=[pl.BlockSpec(memory_space=pl.ANY) for _ in pieces] + [pl.BlockSpec(memory_space=pl.ANY)],
        out_specs=pl.BlockSpec(out_shape, lambda i, *_: (0, 0, 0, 0, 0)),
        scratch_shapes=[
            pltpu.VMEM((total, angles, width), pieces[0].dtype),
            pltpu.VMEM((2, BLOCK) + tiles.shape[1:], tiles.dtype),
            pltpu.VMEM((groups * obs_dev + 1, angles, width), jnp.float32),
            pltpu.SemaphoreType.DMA((len(pieces) + 2,)),
        ],
    )
    return pl.pallas_call(
        field_kernel,
        grid_spec=grid_spec,
        out_shape=jax.ShapeDtypeStruct(out_shape, jnp.float32),
        compiler_params=pltpu.CompilerParams(dimension_semantics=("arbitrary",)),
    )(tile_index, tile_obs, *pieces, tiles)


def shift_pairs(rows, cols, step, along_cols):
    pairs = []
    for a in range(rows):
        for b in range(cols):
            if along_cols:
                pairs.append((a * cols + b, a * cols + (b + step) % cols))
            else:
                pairs.append((a * cols + b, ((a + step) % rows) * cols + b))
    return pairs


def ring_gather(x, rows, cols, along_cols, pieces=False):
    n = cols if along_cols else rows
    plus = shift_pairs(rows, cols, 1, along_cols)
    minus = shift_pairs(rows, cols, -1, along_cols)
    from_behind = lax.ppermute(x, "grp", plus)
    from_ahead = lax.ppermute(x, "grp", minus)
    assert n == 4
    half = x.shape[0] // 2
    far_a = lax.ppermute(from_behind[:half], "grp", plus)
    far_b = lax.ppermute(from_ahead[half:], "grp", minus)
    if pieces:
        return [x, from_ahead, far_a, far_b, from_behind]
    far = jnp.concatenate([far_a, far_b], axis=0)
    return jnp.stack([x, from_ahead, far, from_behind])


def body(history, tiles, tile_src, tile_obs, tile_lag, incident, near_inverse):
    n_grp = lax.axis_size("grp")
    n_lag = lax.axis_size("lag")
    obs_dev, ang_dev, width = incident.shape
    observers = obs_dev * n_grp
    lag_count, src_dev, angles, _ = history.shape
    rows = 4
    cols = n_grp // rows
    assert lag_count == 2 and rows * cols == n_grp
    first = ring_gather(ring_gather(history[0].astype(jnp.bfloat16), rows, cols, True), rows, cols, False, pieces=True)
    second = ring_gather(ring_gather(history[1].astype(jnp.bfloat16), rows, cols, False), rows, cols, True, pieces=True)
    tables = [p.reshape(-1, angles, width) for p in first + second]
    me = lax.axis_index("grp")
    owner = tile_src // src_dev
    local = tile_src % src_dev
    dy = (owner // cols - me // cols + rows) % rows
    dz = (owner % cols - me % cols + cols) % cols
    outer = jnp.where(tile_lag == 0, dy, dz)
    inner = jnp.where(tile_lag == 0, dz, dy)
    upper = (outer == 2) & (inner >= 2)
    piece = jnp.where(outer == 3, 4, outer + upper.astype(outer.dtype))
    source = piece + 5 * tile_lag
    starts = [0]
    for table in tables[:-1]:
        starts.append(starts[-1] + table.shape[0])
    start = jnp.asarray(starts, jnp.int32)[source]
    tile_index = start + (inner - 2 * upper.astype(inner.dtype)) * src_dev + local
    partial = field_partial(tables, tile_index, tile_obs, tiles, n_grp, n_lag, obs_dev)
    partial = partial.reshape(n_grp * n_lag, obs_dev, ang_dev, width)
    received = lax.all_to_all(partial, ("lag", "grp"), 0, 0, tiled=True)
    field = jnp.sum(received, axis=0)
    rhs = (incident - field).astype(jnp.bfloat16)
    new_current = jnp.einsum("oag,ohg->oah", rhs, near_inverse, preferred_element_type=jnp.float32)
    return (field, new_current)


def solution(mesh):
    return jax.shard_map(
        body,
        mesh=mesh,
        in_specs=(
            P("lag", "grp", None, None),
            P(("grp", "lag"), None, None),
            P(("grp", "lag")),
            P(("grp", "lag")),
            P(("grp", "lag")),
            P("grp", "lag", None),
            P("grp", None, None),
        ),
        out_specs=(P("grp", "lag", None), P("grp", "lag", None)),
        check_vma=False,
    )
```
